1024 devices in a mesh: rep: 4 (over z_hi, core), fsdp: 256 (over y, z_lo, x).
Axes of the slice: x: 4, y: 8, z: 16 (z_hi: 2, z_lo: 8; z = z_hi * 8 + z_lo), core: 2. Of those that a mesh axis runs over, the one named last changes fastest.
Arguments:
- anchor: float32 [3584, 7168], P('fsdp'), may hold values from -6 to 6
- momentum: float32 [3584, 7168], P('fsdp', 'rep'), may hold values from -3 to 3
- inner_weight: float32 [4, 3584, 7168], P('rep', 'fsdp'), may hold values from -6 to 6
- first_moment: float32 [4, 3584, 7168], P('rep', 'fsdp'), may hold values from -2 to 2
- second_moment: float32 [4, 3584, 7168], P('rep', 'fsdp'), may hold values from 0.01 to 1
- grad_first: bfloat16 [4, 3584, 7168], P('rep', 'fsdp'), may hold values from -1100 to 1100
- grad_second: bfloat16 [4, 3584, 7168], P('rep', 'fsdp'), may hold values from -1100 to 1100
- outer_step: int32 [1], replicated, may hold values from 0 to 15
Outputs:
- next_anchor: float32 [3584, 7168], P('fsdp')
- next_momentum: float32 [3584, 7168], P('fsdp', 'rep')
- next_inner: float32 [4, 3584, 7168], P('rep', 'fsdp')
- next_first: float32 [4, 3584, 7168], P('rep', 'fsdp')
- next_second: float32 [4, 3584, 7168], P('rep', 'fsdp')
The draws below stay inside these ranges and needn't reach their ends.
All inputs are finite; a program needn't handle non-finite values.
Results may differ from the reference program's by a relative error of at most 0.0003.
Values sent between devices are 32-bit elements; how exact they have to be, the bound alone decides.
No kernel may reach another device: no remote copies, remote signals or barrier semaphores. Data moves between devices by JAX's collectives and lax.ppermute only.
A program may use at most 32 MiB of HBM per device.

```python
import math
import jax
import jax.numpy as jnp

D = 3584
FF = 7168
REPS = 4
N_REP = 4


def grad_draw(key):
    subkeys = jax.random.split(key, 3)
    row_pos = jnp.arange(D, dtype=jnp.float32) / max(D - 1, 1)
    entries = jnp.clip(jax.random.normal(subkeys[0], (REPS, D, FF), jnp.float32), -4.0, 4.0)
    rising = 3.0
    row_scale = jnp.exp(jax.random.uniform(subkeys[1], (REPS, D, 1), jnp.float32) * math.log(10.0))
    row_scale = row_scale * jnp.power(rising, 0.5 * row_pos)[None, :, None]
    col_scale = jnp.exp(jax.random.uniform(subkeys[2], (REPS, 1, FF), jnp.float32) * math.log(10.0))
    return (entries * row_scale * col_scale).astype(jnp.bfloat16)


def draw_grad_first(key, part):
    return grad_draw(jax.random.fold_in(key, 11))


def draw_grad_second(key, part):
    return grad_draw(jax.random.fold_in(key, 12))


def levels(rng, extent, pieces, least, largest):
    def one(dim, blocks):
        heights = jax.random.uniform(jax.random.fold_in(jax.random.fold_in(rng, 6), dim), (blocks,), jnp.float32, least / len(pieces), largest / len(pieces))
        return jnp.repeat(jnp.exp(heights), extent[dim] // blocks).reshape((-1,) + (1,) * (len(extent) - dim - 1))

    level = one(*pieces[0])
    for cut in pieces[1:]:
        level = level * one(*cut)
    return level


def bell_draw(stream_key, shape, spread, reach, pieces=(), kind=jnp.bfloat16):
    gain = levels(stream_key, shape, pieces, -0.22, 0.18) if pieces else 1.0
    result = jax.random.normal(stream_key, shape, jnp.float32) * spread * gain
    return jnp.minimum(jnp.maximum(result, -reach), reach).astype(kind)


def setup_inputs(seed: int = 0) -> dict:
    seeds = jax.random.split(jax.random.key(seed), 9)
    return {
        "anchor": bell_draw(seeds[0], (D, FF), 1.0, 6.0, ((0, 256),), jnp.float32),
        "momentum": bell_draw(seeds[1], (D, FF), 0.5, 3.0, ((0, 256), (1, 4)), jnp.float32),
        "inner_weight": bell_draw(seeds[2], (REPS, D, FF), 1.0, 6.0, ((0, 4), (1, 256)), jnp.float32),
        "first_moment": bell_draw(seeds[3], (REPS, D, FF), 0.3, 2.0, ((0, 4), (1, 256)), jnp.float32),
        "second_moment": jnp.clip(jnp.exp(math.log(1.0) - 4.6051702 * jax.random.uniform(seeds[4], (REPS, D, FF), jnp.float32) ** levels(seeds[4], (REPS, D, FF), ((0, 4), (1, 256)), -0.2, 0.2)), 0.01, 1.0),
        "grad_first": draw_grad_first(jax.random.fold_in(seeds[8], 71), 0),
        "grad_second": draw_grad_second(jax.random.fold_in(seeds[8], 71), 0),
        "outer_step": jax.random.randint(seeds[7], (1,), 0, 16).astype(jnp.int32),
    }


def adam_step(weight, first_moment, second_moment, gradient, step_count):
    grad_full = gradient.astype(jnp.float32)
    square_sum = jnp.sum(grad_full * grad_full)
    factor = jnp.minimum(1.0, 0.5 * math.sqrt(D * FF) / (jnp.sqrt(square_sum) + 1e-06))
    scaled = factor * grad_full
    first_moment = 0.9 * first_moment + 0.1 * scaled
    second_moment = 0.95 * second_moment + 0.05 * scaled * scaled
    first_hat = first_moment / (1.0 - jnp.power(jnp.float32(0.9), step_count))
    second_hat = second_moment / (1.0 - jnp.power(jnp.float32(0.95), step_count))
    weight = weight - 0.1 * (first_hat / (jnp.sqrt(second_hat) + 1e-08) + 0.1 * weight)
    return (weight, first_moment, second_moment)

def reference(anchor, momentum, inner_weight, first_moment, second_moment, grad_first, grad_second, outer_step):
    pseudo_sum = jnp.zeros_like(anchor)
    for replica in range(N_REP):
        pseudo_sum = pseudo_sum + (anchor - inner_weight[replica])
    outer_grad = pseudo_sum / N_REP
    next_momentum = 0.9 * momentum + outer_grad
    next_anchor = anchor - 0.7 * (outer_grad + 0.9 * next_momentum)
    base_step = 2 * outer_step[0]
    inner_list, first_list, second_list = ([], [], [])
    for replica in range(N_REP):
        weight = inner_weight[replica]
        moment_one = first_moment[replica]
        moment_two = second_moment[replica]
        weight, moment_one, moment_two = adam_step(weight, moment_one, moment_two, grad_first[replica], (base_step + 1).astype(jnp.float32))
        weight, moment_one, moment_two = adam_step(weight, moment_one, moment_two, grad_second[replica], (base_step + 2).astype(jnp.float32))
        inner_list.append(next_anchor + (weight - inner_weight[replica]))
        first_list.append(moment_one)
        second_list.append(moment_two)
    return (next_anchor, next_momentum, jnp.stack(inner_list), jnp.stack(first_list), jnp.stack(second_list))
```

```python
import math

import jax
import jax.numpy as jnp
from jax import lax
from jax.sharding import Mesh
from jax.sharding import PartitionSpec as P

D = 3584
FF = 7168
REP = ("z_hi", "core")
FSDP = ("fsdp_0", "fsdp_1", "fsdp_2")


def all_summed(values, axes):
    count = 1
    for axis in axes:
        count *= lax.axis_size(axis)
    spread = jnp.broadcast_to(values[None], (count,) + values.shape)
    return lax.all_to_all(spread, axes, 0, 0, tiled=False).sum(axis=0)


def adam_apply(weight, first_moment, second_moment, grad_full, square_sum, step_count):
    factor = jnp.minimum(1.0, 0.5 * math.sqrt(D * FF) / (jnp.sqrt(square_sum) + 1e-06))
    scaled = factor * grad_full
    first_moment = 0.9 * first_moment + 0.1 * scaled
    second_moment = 0.95 * second_moment + 0.05 * scaled * scaled
    first_hat = first_moment / (1.0 - jnp.power(jnp.float32(0.9), step_count))
    second_hat = second_moment / (1.0 - jnp.power(jnp.float32(0.95), step_count))
    weight = weight - 0.1 * (first_hat / (jnp.sqrt(second_hat) + 1e-08) + 0.1 * weight)
    return (weight, first_moment, second_moment)


def outer_update(anchor, momentum, inner_weight):
    replicas = lax.axis_size("z_hi") * lax.axis_size("core")
    rows, cols = anchor.shape
    block = cols // replicas
    hi = lax.axis_index("z_hi")
    pseudo = (anchor - inner_weight[0]).reshape(rows, 2, 2, block)
    on_chip = lax.all_to_all(pseudo, "core", 2, 2, tiled=True).sum(axis=2)
    payload = jnp.concatenate([on_chip, momentum[:, None, :]], axis=1)
    both = lax.all_gather(payload, "z_hi", axis=0, tiled=False)
    delta_half = both[0, :, :2] + both[1, :, :2]
    outer_grad = delta_half / replicas
    momentum_half = jnp.stack([both[0, :, 2], both[1, :, 2]], axis=1)
    next_momentum = 0.9 * momentum_half + outer_grad
    lo = lax.axis_index("core")
    anchor_half = lax.dynamic_index_in_dim(anchor.reshape(rows, 2, 2, block), lo, 2, keepdims=False)
    anchor_half = anchor_half - 0.7 * (outer_grad + 0.9 * next_momentum)
    next_anchor = lax.all_gather(anchor_half, "core", axis=2, tiled=False).reshape(rows, cols)
    own_momentum = lax.dynamic_index_in_dim(next_momentum, hi, 1, keepdims=False)
    return (next_anchor, own_momentum)


def inner_steps(inner_weight, first_moment, second_moment, grad_first, grad_second, outer_step):
    base_step = 2 * outer_step[0]
    grad_one = grad_first[0].astype(jnp.float32)
    grad_two = grad_second[0].astype(jnp.float32)
    squares = jnp.stack([jnp.sum(grad_one * grad_one), jnp.sum(grad_two * grad_two)])
    norm_one, norm_two = all_summed(squares, FSDP)
    weight, moment_one, moment_two = adam_apply(
        inner_weight[0],
        first_moment[0],
        second_moment[0],
        grad_one,
        norm_one,
        (base_step + 1).astype(jnp.float32),
    )
    weight, moment_one, moment_two = adam_apply(
        weight, moment_one, moment_two, grad_two, norm_two, (base_step + 2).astype(jnp.float32)
    )
    return (weight, moment_one, moment_two)


def on_device(
    anchor, momentum, inner_weight, first_moment, second_moment, grad_first, grad_second, outer_step
):
    weight, moment_one, moment_two = inner_steps(
        inner_weight, first_moment, second_moment, grad_first, grad_second, outer_step
    )
    next_anchor, next_momentum = outer_update(anchor, momentum, inner_weight)
    next_inner = (next_anchor + (weight - inner_weight[0]))[None]
    return (next_anchor, next_momentum, next_inner, moment_one[None], moment_two[None])


def solution(mesh):
    fsdp = mesh.shape["fsdp"]
    split = Mesh(
        mesh.devices.reshape(2, mesh.shape["rep"] // 2, fsdp // 32, 8, 4),
        REP + FSDP,
    )
    return jax.shard_map(
        on_device,
        mesh=split,
        in_specs=(
            P(FSDP, None),
            P(FSDP, REP),
            P(REP, FSDP, None),
            P(REP, FSDP, None),
            P(REP, FSDP, None),
            P(REP, FSDP, None),
            P(REP, FSDP, None),
            P(),
        ),
        out_specs=(
            P(FSDP, None),
            P(FSDP, REP),
            P(REP, FSDP, None),
            P(REP, FSDP, None),
            P(REP, FSDP, None),
        ),
        check_vma=False,
    )
```

```python
import math

import jax
import jax.numpy as jnp
from jax import lax
from jax.sharding import Mesh
from jax.sharding import PartitionSpec as P

D = 3584
FF = 7168
REP = ("z_hi", "core")
FSDP = ("fsdp_0", "fsdp_1", "fsdp_2")


def all_summed(values, axes):
    count = 1
    for axis in axes:
        count *= lax.axis_size(axis)
    spread = jnp.broadcast_to(values[None], (count,) + values.shape)
    return lax.all_to_all(spread, axes, 0, 0, tiled=False).sum(axis=0)


def adam_apply(weight, first_moment, second_moment, grad_full, square_sum, step_count):
    factor = jnp.minimum(1.0, 0.5 * math.sqrt(D * FF) / (jnp.sqrt(square_sum) + 1e-06))
    scaled = factor * grad_full
    first_moment = 0.9 * first_moment + 0.1 * scaled
    second_moment = 0.95 * second_moment + 0.05 * scaled * scaled
    first_hat = first_moment / (1.0 - jnp.power(jnp.float32(0.9), step_count))
    second_hat = second_moment / (1.0 - jnp.power(jnp.float32(0.95), step_count))
    weight = weight - 0.1 * (first_hat / (jnp.sqrt(second_hat) + 1e-08) + 0.1 * weight)
    return (weight, first_moment, second_moment)


def outer_update(anchor, momentum, inner_weight):
    replicas = lax.axis_size("z_hi") * lax.axis_size("core")
    rows, cols = anchor.shape
    block = cols // replicas
    hi = lax.axis_index("z_hi")
    lo = lax.axis_index("core")
    pseudo = (anchor - inner_weight[0]).reshape(rows, 2, 2, block)
    on_chip = lax.all_to_all(pseudo, "core", 2, 2, tiled=True).sum(axis=2)
    anchor_half = lax.dynamic_index_in_dim(anchor.reshape(rows, 2, 2, block), lo, 2, keepdims=False)
    own_sum = lax.dynamic_index_in_dim(on_chip, hi, 1, keepdims=False)
    other_sum = lax.dynamic_index_in_dim(on_chip, 1 - hi, 1, keepdims=False)
    own_anchor = lax.dynamic_index_in_dim(anchor_half, hi, 1, keepdims=False)
    folded = own_anchor - 0.567 * momentum - 0.3325 * own_sum
    payload = jnp.stack([folded, other_sum], axis=1)
    both = lax.all_gather(payload, "z_hi", axis=0, tiled=False)
    anchor_half = jnp.stack(
        [both[0, :, 0] - 0.3325 * both[1, :, 1], both[1, :, 0] - 0.3325 * both[0, :, 1]], axis=1
    )
    next_anchor = lax.all_gather(anchor_half, "core", axis=2, tiled=False).reshape(rows, cols)
    arrived = lax.dynamic_index_in_dim(both, 1 - hi, 0, keepdims=False)[:, 1]
    outer_grad = (own_sum + arrived) / replicas
    next_momentum = 0.9 * momentum + outer_grad
    return (next_anchor, next_momentum)


def inner_steps(inner_weight, first_moment, second_moment, grad_first, grad_second, outer_step):
    base_step = 2 * outer_step[0]
    grad_one = grad_first[0].astype(jnp.float32)
    grad_two = grad_second[0].astype(jnp.float32)
    squares = jnp.stack([jnp.sum(grad_one * grad_one), jnp.sum(grad_two * grad_two)])
    norm_one, norm_two = all_summed(squares, FSDP)
    weight, moment_one, moment_two = adam_apply(
        inner_weight[0],
        first_moment[0],
        second_moment[0],
        grad_one,
        norm_one,
        (base_step + 1).astype(jnp.float32),
    )
    weight, moment_one, moment_two = adam_apply(
        weight, moment_one, moment_two, grad_two, norm_two, (base_step + 2).astype(jnp.float32)
    )
    return (weight, moment_one, moment_two)


def on_device(
    anchor, momentum, inner_weight, first_moment, second_moment, grad_first, grad_second, outer_step
):
    weight, moment_one, moment_two = inner_steps(
        inner_weight, first_moment, second_moment, grad_first, grad_second, outer_step
    )
    next_anchor, next_momentum = outer_update(anchor, momentum, inner_weight)
    next_inner = (next_anchor + (weight - inner_weight[0]))[None]
    return (next_anchor, next_momentum, next_inner, moment_one[None], moment_two[None])


def solution(mesh):
    fsdp = mesh.shape["fsdp"]
    split = Mesh(
        mesh.devices.reshape(2, mesh.shape["rep"] // 2, fsdp // 32, 8, 4),
        REP + FSDP,
    )
    return jax.shard_map(
        on_device,
        mesh=split,
        in_specs=(
            P(FSDP, None),
            P(FSDP, REP),
            P(REP, FSDP, None),
            P(REP, FSDP, None),
            P(REP, FSDP, None),
            P(REP, FSDP, None),
            P(REP, FSDP, None),
            P(),
        ),
        out_specs=(
            P(FSDP, None),
            P(FSDP, REP),
            P(REP, FSDP, None),
            P(REP, FSDP, None),
            P(REP, FSDP, None),
        ),
        check_vma=False,
    )
```

```python
import math

import jax
import jax.numpy as jnp
from jax import lax
from jax.sharding import Mesh
from jax.sharding import PartitionSpec as P

D = 3584
FF = 7168
REP = ("z_hi", "core")
FSDP = ("fsdp_0", "fsdp_1", "fsdp_2")


def all_summed(values, axes):
    count = 1
    for axis in axes:
        count *= lax.axis_size(axis)
    spread = jnp.broadcast_to(values[None], (count,) + values.shape)
    return lax.all_to_all(spread, axes, 0, 0, tiled=False).sum(axis=0)


def adam_apply(weight, first_moment, second_moment, grad_full, square_sum, step_count):
    factor = jnp.minimum(1.0, 0.5 * math.sqrt(D * FF) / (jnp.sqrt(square_sum) + 1e-06))
    scaled = factor * grad_full
    first_moment = 0.9 * first_moment + 0.1 * scaled
    second_moment = 0.95 * second_moment + 0.05 * scaled * scaled
    first_hat = first_moment / (1.0 - jnp.power(jnp.float32(0.9), step_count))
    second_hat = second_moment / (1.0 - jnp.power(jnp.float32(0.95), step_count))
    weight = weight - 0.1 * (first_hat / (jnp.sqrt(second_hat) + 1e-08) + 0.1 * weight)
    return (weight, first_moment, second_moment)


def outer_update(anchor, momentum, inner_weight):
    replicas = lax.axis_size("z_hi") * lax.axis_size("core")
    rows, cols = anchor.shape
    block = cols // replicas
    hi = lax.axis_index("z_hi")
    lo = lax.axis_index("core")
    pseudo = (anchor - inner_weight[0]).reshape(rows, 2, 2, block)
    on_chip = lax.all_to_all(pseudo, "core", 2, 2, tiled=True).sum(axis=2)
    anchor_half = lax.dynamic_index_in_dim(anchor.reshape(rows, 2, 2, block), lo, 2, keepdims=False)
    own_sum = lax.dynamic_index_in_dim(on_chip, hi, 1, keepdims=False)
    other_sum = lax.dynamic_index_in_dim(on_chip, 1 - hi, 1, keepdims=False)
    own_anchor = lax.dynamic_index_in_dim(anchor_half, hi, 1, keepdims=False)
    folded = own_anchor - 0.567 * momentum - 0.3325 * own_sum
    payload = jnp.stack([folded, other_sum], axis=1)
    arrived = lax.ppermute(payload, "z_hi", [(0, 1), (1, 0)])
    mine = folded - 0.3325 * arrived[:, 1]
    theirs = arrived[:, 0] - 0.3325 * other_sum
    anchor_half = jnp.where(hi == 0, jnp.stack([mine, theirs], axis=1), jnp.stack([theirs, mine], axis=1))
    next_anchor = lax.all_gather(anchor_half, "core", axis=2, tiled=False).reshape(rows, cols)
    outer_grad = (own_sum + arrived[:, 1]) / replicas
    next_momentum = 0.9 * momentum + outer_grad
    return (next_anchor, next_momentum)


def inner_steps(inner_weight, first_moment, second_moment, grad_first, grad_second, outer_step):
    base_step = 2 * outer_step[0]
    grad_one = grad_first[0].astype(jnp.float32)
    grad_two = grad_second[0].astype(jnp.float32)
    squares = jnp.stack([jnp.sum(grad_one * grad_one), jnp.sum(grad_two * grad_two)])
    norm_one, norm_two = all_summed(squares, FSDP)
    weight, moment_one, moment_two = adam_apply(
        inner_weight[0],
        first_moment[0],
        second_moment[0],
        grad_one,
        norm_one,
        (base_step + 1).astype(jnp.float32),
    )
    weight, moment_one, moment_two = adam_apply(
        weight, moment_one, moment_two, grad_two, norm_two, (base_step + 2).astype(jnp.float32)
    )
    return (weight, moment_one, moment_two)


def on_device(
    anchor, momentum, inner_weight, first_moment, second_moment, grad_first, grad_second, outer_step
):
    weight, moment_one, moment_two = inner_steps(
        inner_weight, first_moment, second_moment, grad_first, grad_second, outer_step
    )
    next_anchor, next_momentum = outer_update(anchor, momentum, inner_weight)
    next_inner = (next_anchor + (weight - inner_weight[0]))[None]
    return (next_anchor, next_momentum, next_inner, moment_one[None], moment_two[None])


def solution(mesh):
    fsdp = mesh.shape["fsdp"]
    split = Mesh(
        mesh.devices.reshape(2, mesh.shape["rep"] // 2, fsdp // 32, 8, 4),
        REP + FSDP,
    )
    return jax.shard_map(
        on_device,
        mesh=split,
        in_specs=(
            P(FSDP, None),
            P(FSDP, REP),
            P(REP, FSDP, None),
            P(REP, FSDP, None),
            P(REP, FSDP, None),
            P(REP, FSDP, None),
            P(REP, FSDP, None),
            P(),
        ),
        out_specs=(
            P(FSDP, None),
            P(FSDP, REP),
            P(REP, FSDP, None),
            P(REP, FSDP, None),
            P(REP, FSDP, None),
        ),
        check_vma=False,
    )
```

```python
import math

import jax
import jax.numpy as jnp
from jax import lax
from jax.sharding import Mesh
from jax.sharding import PartitionSpec as P

D = 3584
FF = 7168
REP = ("z_hi", "core")
FSDP = ("fsdp_0", "fsdp_1", "fsdp_2")


def all_summed(values, axes):
    count = 1
    for axis in axes:
        count *= lax.axis_size(axis)
    spread = jnp.broadcast_to(values[None], (count,) + values.shape)
    return lax.all_to_all(spread, axes, 0, 0, tiled=False).sum(axis=0)


def adam_apply(weight, first_moment, second_moment, grad_full, square_sum, step_count):
    factor = jnp.minimum(1.0, 0.5 * math.sqrt(D * FF) / (jnp.sqrt(square_sum) + 1e-06))
    scaled = factor * grad_full
    first_moment = 0.9 * first_moment + 0.1 * scaled
    second_moment = 0.95 * second_moment + 0.05 * scaled * scaled
    first_hat = first_moment / (1.0 - jnp.power(jnp.float32(0.9), step_count))
    second_hat = second_moment / (1.0 - jnp.power(jnp.float32(0.95), step_count))
    weight = weight - 0.1 * (first_hat / (jnp.sqrt(second_hat) + 1e-08) + 0.1 * weight)
    return (weight, first_moment, second_moment)


def outer_update(anchor, momentum, inner_weight):
    replicas = lax.axis_size("z_hi") * lax.axis_size("core")
    rows, cols = anchor.shape
    block = cols // replicas
    hi = lax.axis_index("z_hi")
    lo = lax.axis_index("core")
    pseudo = (anchor - inner_weight[0]).reshape(rows, 2, 2, block)
    kept = lax.dynamic_index_in_dim(pseudo, lo, 2, keepdims=False)
    given = lax.dynamic_index_in_dim(pseudo, 1 - lo, 2, keepdims=False)
    on_chip = kept + lax.ppermute(given, "core", [(0, 1), (1, 0)])
    anchor_half = lax.dynamic_index_in_dim(anchor.reshape(rows, 2, 2, block), lo, 2, keepdims=False)
    own_sum = lax.dynamic_index_in_dim(on_chip, hi, 1, keepdims=False)
    other_sum = lax.dynamic_index_in_dim(on_chip, 1 - hi, 1, keepdims=False)
    own_anchor = lax.dynamic_index_in_dim(anchor_half, hi, 1, keepdims=False)
    folded = own_anchor - 0.567 * momentum - 0.3325 * own_sum
    payload = jnp.stack([folded, other_sum], axis=1)
    both = lax.all_gather(payload, "z_hi", axis=0, tiled=False)
    anchor_half = jnp.stack(
        [both[0, :, 0] - 0.3325 * both[1, :, 1], both[1, :, 0] - 0.3325 * both[0, :, 1]], axis=1
    )
    next_anchor = lax.all_gather(anchor_half, "core", axis=2, tiled=False).reshape(rows, cols)
    arrived = lax.dynamic_index_in_dim(both, 1 - hi, 0, keepdims=False)[:, 1]
    outer_grad = (own_sum + arrived) / replicas
    next_momentum = 0.9 * momentum + outer_grad
    return (next_anchor, next_momentum)


def inner_steps(inner_weight, first_moment, second_moment, grad_first, grad_second, outer_step):
    base_step = 2 * outer_step[0]
    grad_one = grad_first[0].astype(jnp.float32)
    grad_two = grad_second[0].astype(jnp.float32)
    both_grads = jnp.stack([grad_one, grad_two])
    squares = jnp.sum(both_grads * both_grads, axis=(1, 2))
    norm_one, norm_two = all_summed(squares, FSDP)
    weight, moment_one, moment_two = adam_apply(
        inner_weight[0],
        first_moment[0],
        second_moment[0],
        grad_one,
        norm_one,
        (base_step + 1).astype(jnp.float32),
    )
    weight, moment_one, moment_two = adam_apply(
        weight, moment_one, moment_two, grad_two, norm_two, (base_step + 2).astype(jnp.float32)
    )
    return (weight, moment_one, moment_two)


def on_device(
    anchor, momentum, inner_weight, first_moment, second_moment, grad_first, grad_second, outer_step
):
    weight, moment_one, moment_two = inner_steps(
        inner_weight, first_moment, second_moment, grad_first, grad_second, outer_step
    )
    next_anchor, next_momentum = outer_update(anchor, momentum, inner_weight)
    next_inner = (next_anchor + (weight - inner_weight[0]))[None]
    return (next_anchor, next_momentum, next_inner, moment_one[None], moment_two[None])


def solution(mesh):
    fsdp = mesh.shape["fsdp"]
    split = Mesh(
        mesh.devices.reshape(2, mesh.shape["rep"] // 2, fsdp // 32, 8, 4),
        REP + FSDP,
    )
    return jax.shard_map(
        on_device,
        mesh=split,
        in_specs=(
            P(FSDP, None),
            P(FSDP, REP),
            P(REP, FSDP, None),
            P(REP, FSDP, None),
            P(REP, FSDP, None),
            P(REP, FSDP, None),
            P(REP, FSDP, None),
            P(),
        ),
        out_specs=(
            P(FSDP, None),
            P(FSDP, REP),
            P(REP, FSDP, None),
            P(REP, FSDP, None),
            P(REP, FSDP, None),
        ),
        check_vma=False,
    )
```

```python
import math

import jax
import jax.numpy as jnp
from jax import lax
from jax.sharding import Mesh
from jax.sharding import PartitionSpec as P

D = 3584
FF = 7168
REP = ("z_hi", "core")
FSDP = ("fsdp_0", "fsdp_1", "fsdp_2")


def all_summed(values, axes):
    count = 1
    for axis in axes:
        count *= lax.axis_size(axis)
    spread = jnp.broadcast_to(values[None], (count,) + values.shape)
    return lax.all_to_all(spread, axes, 0, 0, tiled=False).sum(axis=0)


def adam_apply(weight, first_moment, second_moment, grad_full, square_sum, step_count):
    factor = jnp.minimum(1.0, 0.5 * math.sqrt(D * FF) / (jnp.sqrt(square_sum) + 1e-06))
    scaled = factor * grad_full
    first_moment = 0.9 * first_moment + 0.1 * scaled
    second_moment = 0.95 * second_moment + 0.05 * scaled * scaled
    first_hat = first_moment / (1.0 - jnp.power(jnp.float32(0.9), step_count))
    second_hat = second_moment / (1.0 - jnp.power(jnp.float32(0.95), step_count))
    weight = weight - 0.1 * (first_hat / (jnp.sqrt(second_hat) + 1e-08) + 0.1 * weight)
    return (weight, first_moment, second_moment)


def outer_update(anchor, momentum, inner_weight):
    replicas = lax.axis_size("z_hi") * lax.axis_size("core")
    rows, cols = anchor.shape
    block = cols // replicas
    hi = lax.axis_index("z_hi")
    lo = lax.axis_index("core")
    pseudo = (anchor - inner_weight[0]).reshape(rows, 2, 2, block)
    on_chip = lax.all_to_all(pseudo, "core", 2, 2, tiled=True).sum(axis=2)
    anchor_half = lax.dynamic_index_in_dim(anchor.reshape(rows, 2, 2, block), lo, 2, keepdims=False)
    own_sum = lax.dynamic_index_in_dim(on_chip, hi, 1, keepdims=False)
    other_sum = lax.dynamic_index_in_dim(on_chip, 1 - hi, 1, keepdims=False)
    own_anchor = lax.dynamic_index_in_dim(anchor_half, hi, 1, keepdims=False)
    folded = own_anchor - 0.567 * momentum - 0.3325 * own_sum
    payload = jnp.stack([folded, other_sum], axis=1)
    both = lax.all_gather(payload, "z_hi", axis=0, tiled=False)
    anchor_half = jnp.stack(
        [both[0, :, 0] - 0.3325 * both[1, :, 1], both[1, :, 0] - 0.3325 * both[0, :, 1]], axis=1
    )
    next_anchor = lax.all_gather(anchor_half, "core", axis=2, tiled=False).reshape(rows, cols)
    arrived = lax.dynamic_index_in_dim(both, 1 - hi, 0, keepdims=False)[:, 1]
    outer_grad = (own_sum + arrived) / replicas
    next_momentum = 0.9 * momentum + outer_grad
    return (next_anchor, next_momentum)


def inner_steps(inner_weight, first_moment, second_moment, grad_first, grad_second, outer_step):
    base_step = 2 * outer_step[0]
    grad_one = grad_first[0].astype(jnp.float32)
    grad_two = grad_second[0].astype(jnp.float32)
    both_grads = jnp.stack([grad_one, grad_two])
    squares = jnp.sum(both_grads * both_grads, axis=(1, 2))
    norm_one, norm_two = all_summed(squares, FSDP)
    weight, moment_one, moment_two = adam_apply(
        inner_weight[0],
        first_moment[0],
        second_moment[0],
        grad_one,
        norm_one,
        (base_step + 1).astype(jnp.float32),
    )
    weight, moment_one, moment_two = adam_apply(
        weight, moment_one, moment_two, grad_two, norm_two, (base_step + 2).astype(jnp.float32)
    )
    return (weight, moment_one, moment_two)


def on_device(
    anchor, momentum, inner_weight, first_moment, second_moment, grad_first, grad_second, outer_step
):
    weight, moment_one, moment_two = inner_steps(
        inner_weight, first_moment, second_moment, grad_first, grad_second, outer_step
    )
    next_anchor, next_momentum = outer_update(anchor, momentum, inner_weight)
    next_inner = (next_anchor + (weight - inner_weight[0]))[None]
    return (next_anchor, next_momentum, next_inner, moment_one[None], moment_two[None])


def solution(mesh):
    fsdp = mesh.shape["fsdp"]
    split = Mesh(
        mesh.devices.reshape(2, mesh.shape["rep"] // 2, fsdp // 32, 8, 4),
        REP + FSDP,
    )
    return jax.shard_map(
        on_device,
        mesh=split,
        in_specs=(
            P(FSDP, None),
            P(FSDP, REP),
            P(REP, FSDP, None),
            P(REP, FSDP, None),
            P(REP, FSDP, None),
            P(REP, FSDP, None),
            P(REP, FSDP, None),
            P(),
        ),
        out_specs=(
            P(FSDP, None),
            P(FSDP, REP),
            P(REP, FSDP, None),
            P(REP, FSDP, None),
            P(REP, FSDP, None),
        ),
        check_vma=False,
    )
```

```python
import math

import jax
import jax.numpy as jnp
from jax import lax
from jax.sharding import Mesh
from jax.sharding import PartitionSpec as P

D = 3584
FF = 7168
REP = ("z_hi", "core")
FSDP = ("fsdp_0", "fsdp_1", "fsdp_2")


def all_summed(values, axes):
    count = 1
    for axis in axes:
        count *= lax.axis_size(axis)
    spread = jnp.broadcast_to(values[None], (count,) + values.shape)
    return lax.all_to_all(spread, axes, 0, 0, tiled=False).sum(axis=0)


def adam_apply(weight, first_moment, second_moment, grad_full, square_sum, step_count):
    factor = jnp.minimum(1.0, 0.5 * math.sqrt(D * FF) / (jnp.sqrt(square_sum) + 1e-06))
    scaled = factor * grad_full
    first_moment = 0.9 * first_moment + 0.1 * scaled
    second_moment = 0.95 * second_moment + 0.05 * scaled * scaled
    first_hat = first_moment / (1.0 - jnp.power(jnp.float32(0.9), step_count))
    second_hat = second_moment / (1.0 - jnp.power(jnp.float32(0.95), step_count))
    weight = weight - 0.1 * (first_hat / (jnp.sqrt(second_hat) + 1e-08) + 0.1 * weight)
    return (weight, first_moment, second_moment)


def outer_update(anchor, momentum, inner_weight):
    replicas = lax.axis_size("z_hi") * lax.axis_size("core")
    rows, cols = anchor.shape
    block = cols // replicas
    hi = lax.axis_index("z_hi")
    lo = lax.axis_index("core")
    pseudo = (anchor - inner_weight[0]).reshape(rows, 2, 2, block)
    kept = lax.dynamic_index_in_dim(pseudo, lo, 2, keepdims=False)
    given = lax.dynamic_index_in_dim(pseudo, 1 - lo, 2, keepdims=False)
    from_sibling = lax.dynamic_index_in_dim(
        lax.all_gather(given, "core", axis=0, tiled=False), 1 - lo, 0, keepdims=False
    )
    on_chip = kept + from_sibling
    anchor_half = lax.dynamic_index_in_dim(anchor.reshape(rows, 2, 2, block), lo, 2, keepdims=False)
    own_sum = lax.dynamic_index_in_dim(on_chip, hi, 1, keepdims=False)
    other_sum = lax.dynamic_index_in_dim(on_chip, 1 - hi, 1, keepdims=False)
    own_anchor = lax.dynamic_index_in_dim(anchor_half, hi, 1, keepdims=False)
    folded = own_anchor - 0.567 * momentum - 0.3325 * own_sum
    payload = jnp.stack([folded, other_sum], axis=1)
    both = lax.all_gather(payload, "z_hi", axis=0, tiled=False)
    anchor_half = jnp.stack(
        [both[0, :, 0] - 0.3325 * both[1, :, 1], both[1, :, 0] - 0.3325 * both[0, :, 1]], axis=1
    )
    next_anchor = lax.all_gather(anchor_half, "core", axis=2, tiled=False).reshape(rows, cols)
    arrived = lax.dynamic_index_in_dim(both, 1 - hi, 0, keepdims=False)[:, 1]
    outer_grad = (own_sum + arrived) / replicas
    next_momentum = 0.9 * momentum + outer_grad
    return (next_anchor, next_momentum)


def inner_steps(inner_weight, first_moment, second_moment, grad_first, grad_second, outer_step):
    base_step = 2 * outer_step[0]
    grad_one = grad_first[0].astype(jnp.float32)
    grad_two = grad_second[0].astype(jnp.float32)
    both_grads = jnp.stack([grad_one, grad_two])
    squares = jnp.sum(both_grads * both_grads, axis=(1, 2))
    norm_one, norm_two = all_summed(squares, FSDP)
    weight, moment_one, moment_two = adam_apply(
        inner_weight[0],
        first_moment[0],
        second_moment[0],
        grad_one,
        norm_one,
        (base_step + 1).astype(jnp.float32),
    )
    weight, moment_one, moment_two = adam_apply(
        weight, moment_one, moment_two, grad_two, norm_two, (base_step + 2).astype(jnp.float32)
    )
    return (weight, moment_one, moment_two)


def on_device(
    anchor, momentum, inner_weight, first_moment, second_moment, grad_first, grad_second, outer_step
):
    weight, moment_one, moment_two = inner_steps(
        inner_weight, first_moment, second_moment, grad_first, grad_second, outer_step
    )
    next_anchor, next_momentum = outer_update(anchor, momentum, inner_weight)
    next_inner = (next_anchor + (weight - inner_weight[0]))[None]
    return (next_anchor, next_momentum, next_inner, moment_one[None], moment_two[None])


def solution(mesh):
    fsdp = mesh.shape["fsdp"]
    split = Mesh(
        mesh.devices.reshape(2, mesh.shape["rep"] // 2, fsdp // 32, 8, 4),
        REP + FSDP,
    )
    return jax.shard_map(
        on_device,
        mesh=split,
        in_specs=(
            P(FSDP, None),
            P(FSDP, REP),
            P(REP, FSDP, None),
            P(REP, FSDP, None),
            P(REP, FSDP, None),
            P(REP, FSDP, None),
            P(REP, FSDP, None),
            P(),
        ),
        out_specs=(
            P(FSDP, None),
            P(FSDP, REP),
            P(REP, FSDP, None),
            P(REP, FSDP, None),
            P(REP, FSDP, None),
        ),
        check_vma=False,
    )
```

```python
import math

import jax
import jax.numpy as jnp
from jax import lax
from jax.sharding import Mesh
from jax.sharding import PartitionSpec as P

D = 3584
FF = 7168
REP = ("z_hi", "core")
FSDP = ("fsdp_0", "fsdp_1", "fsdp_2")


def all_summed(values, axes):
    count = 1
    for axis in axes:
        count *= lax.axis_size(axis)
    spread = jnp.broadcast_to(values[None], (count,) + values.shape)
    return lax.all_to_all(spread, axes, 0, 0, tiled=False).sum(axis=0)


def adam_apply(weight, first_moment, second_moment, grad_full, square_sum, step_count):
    factor = jnp.minimum(1.0, 0.5 * math.sqrt(D * FF) / (jnp.sqrt(square_sum) + 1e-06))
    scaled = factor * grad_full
    first_moment = 0.9 * first_moment + 0.1 * scaled
    second_moment = 0.95 * second_moment + 0.05 * scaled * scaled
    first_hat = first_moment / (1.0 - jnp.power(jnp.float32(0.9), step_count))
    second_hat = second_moment / (1.0 - jnp.power(jnp.float32(0.95), step_count))
    weight = weight - 0.1 * (first_hat / (jnp.sqrt(second_hat) + 1e-08) + 0.1 * weight)
    return (weight, first_moment, second_moment)


def outer_update(anchor, momentum, inner_weight):
    replicas = lax.axis_size("z_hi") * lax.axis_size("core")
    rows, cols = anchor.shape
    block = cols // replicas
    hi = lax.axis_index("z_hi")
    lo = lax.axis_index("core")
    pseudo = (anchor - inner_weight[0]).reshape(rows, 2, 2, block)
    kept = lax.dynamic_index_in_dim(pseudo, lo, 2, keepdims=False)
    given = lax.dynamic_index_in_dim(pseudo, 1 - lo, 2, keepdims=False)
    from_sibling = lax.dynamic_index_in_dim(
        lax.all_gather(given, "core", axis=0, tiled=False), 1 - lo, 0, keepdims=False
    )
    on_chip = kept + from_sibling
    anchor_half = lax.dynamic_index_in_dim(anchor.reshape(rows, 2, 2, block), lo, 2, keepdims=False)
    own_sum = lax.dynamic_index_in_dim(on_chip, hi, 1, keepdims=False)
    other_sum = lax.dynamic_index_in_dim(on_chip, 1 - hi, 1, keepdims=False)
    own_anchor = lax.dynamic_index_in_dim(anchor_half, hi, 1, keepdims=False)
    folded = own_anchor - 0.567 * momentum - 0.3325 * own_sum
    payload = jnp.stack([folded, other_sum], axis=1)
    every = lax.all_gather(payload, REP, axis=0, tiled=False).reshape(2, 2, rows, 2, block)
    next_anchor = jnp.stack(
        [
            jnp.stack(
                [every[h, c, :, 0] - 0.3325 * every[1 - h, c, :, 1] for c in range(2)], axis=1
            )
            for h in range(2)
        ],
        axis=1,
    ).reshape(rows, cols)
    partner = lax.dynamic_index_in_dim(every, 1 - hi, 0, keepdims=False)
    arrived = lax.dynamic_index_in_dim(partner, lo, 0, keepdims=False)[:, 1]
    outer_grad = (own_sum + arrived) / replicas
    next_momentum = 0.9 * momentum + outer_grad
    return (next_anchor, next_momentum)


def inner_steps(inner_weight, first_moment, second_moment, grad_first, grad_second, outer_step):
    base_step = 2 * outer_step[0]
    grad_one = grad_first[0].astype(jnp.float32)
    grad_two = grad_second[0].astype(jnp.float32)
    both_grads = jnp.stack([grad_one, grad_two])
    squares = jnp.sum(both_grads * both_grads, axis=(1, 2))
    norm_one, norm_two = all_summed(squares, FSDP)
    weight, moment_one, moment_two = adam_apply(
        inner_weight[0],
        first_moment[0],
        second_moment[0],
        grad_one,
        norm_one,
        (base_step + 1).astype(jnp.float32),
    )
    weight, moment_one, moment_two = adam_apply(
        weight, moment_one, moment_two, grad_two, norm_two, (base_step + 2).astype(jnp.float32)
    )
    return (weight, moment_one, moment_two)


def on_device(
    anchor, momentum, inner_weight, first_moment, second_moment, grad_first, grad_second, outer_step
):
    weight, moment_one, moment_two = inner_steps(
        inner_weight, first_moment, second_moment, grad_first, grad_second, outer_step
    )
    next_anchor, next_momentum = outer_update(anchor, momentum, inner_weight)
    next_inner = (next_anchor + (weight - inner_weight[0]))[None]
    return (next_anchor, next_momentum, next_inner, moment_one[None], moment_two[None])


def solution(mesh):
    fsdp = mesh.shape["fsdp"]
    split = Mesh(
        mesh.devices.reshape(2, mesh.shape["rep"] // 2, fsdp // 32, 8, 4),
        REP + FSDP,
    )
    return jax.shard_map(
        on_device,
        mesh=split,
        in_specs=(
            P(FSDP, None),
            P(FSDP, REP),
            P(REP, FSDP, None),
            P(REP, FSDP, None),
            P(REP, FSDP, None),
            P(REP, FSDP, None),
            P(REP, FSDP, None),
            P(),
        ),
        out_specs=(
            P(FSDP, None),
            P(FSDP, REP),
            P(REP, FSDP, None),
            P(REP, FSDP, None),
            P(REP, FSDP, None),
        ),
        check_vma=False,
    )
```

```python
import math

import jax
import jax.numpy as jnp
from jax import lax
from jax.sharding import Mesh
from jax.sharding import PartitionSpec as P

D = 3584
FF = 7168
REP = ("z_hi", "core")
FSDP = ("fsdp_0", "fsdp_1", "fsdp_2")


def all_summed(values, axes):
    count = 1
    for axis in axes:
        count *= lax.axis_size(axis)
    spread = jnp.broadcast_to(values[None], (count,) + values.shape)
    return lax.all_to_all(spread, axes, 0, 0, tiled=False).sum(axis=0)


def adam_apply(weight, first_moment, second_moment, grad_full, square_sum, step_count):
    factor = jnp.minimum(1.0, 0.5 * math.sqrt(D * FF) / (jnp.sqrt(square_sum) + 1e-06))
    scaled = factor * grad_full
    first_moment = 0.9 * first_moment + 0.1 * scaled
    second_moment = 0.95 * second_moment + 0.05 * scaled * scaled
    first_hat = first_moment / (1.0 - jnp.power(jnp.float32(0.9), step_count))
    second_hat = second_moment / (1.0 - jnp.power(jnp.float32(0.95), step_count))
    weight = weight - 0.1 * (first_hat / (jnp.sqrt(second_hat) + 1e-08) + 0.1 * weight)
    return (weight, first_moment, second_moment)


def outer_update(anchor, momentum, inner_weight):
    replicas = lax.axis_size("z_hi") * lax.axis_size("core")
    rows, cols = anchor.shape
    block = cols // replicas
    hi = lax.axis_index("z_hi")
    lo = lax.axis_index("core")

    def column(x, b):
        return lax.dynamic_slice_in_dim(x, b * block, block, 1)

    pseudo = anchor - inner_weight[0]
    kept = jnp.concatenate([column(pseudo, lo), column(pseudo, 2 + lo)], axis=1)
    given = jnp.concatenate([column(pseudo, 1 - lo), column(pseudo, 3 - lo)], axis=1)
    sibling = lax.all_gather(given, "core", axis=0, tiled=False)
    on_chip = kept + lax.dynamic_index_in_dim(sibling, 1 - lo, 0, keepdims=False)
    own_sum = column(on_chip, hi)
    other_sum = column(on_chip, 1 - hi)
    folded = column(anchor, 2 * hi + lo) - 0.567 * momentum - 0.3325 * own_sum
    payload = jnp.concatenate([folded, other_sum], axis=1)
    every = lax.all_gather(payload, REP, axis=0, tiled=False)
    next_anchor = jnp.concatenate(
        [
            every[b, :, :block] - 0.3325 * every[(b + 2) % 4, :, block:]
            for b in range(replicas)
        ],
        axis=1,
    )
    arrived = lax.dynamic_index_in_dim(every, 2 * (1 - hi) + lo, 0, keepdims=False)[:, block:]
    outer_grad = (own_sum + arrived) / replicas
    next_momentum = 0.9 * momentum + outer_grad
    return (next_anchor, next_momentum)


def inner_steps(inner_weight, first_moment, second_moment, grad_first, grad_second, outer_step):
    base_step = 2 * outer_step[0]
    grad_one = grad_first[0].astype(jnp.float32)
    grad_two = grad_second[0].astype(jnp.float32)
    both_grads = jnp.stack([grad_one, grad_two])
    squares = jnp.sum(both_grads * both_grads, axis=(1, 2))
    norm_one, norm_two = all_summed(squares, FSDP)
    weight, moment_one, moment_two = adam_apply(
        inner_weight[0],
        first_moment[0],
        second_moment[0],
        grad_one,
        norm_one,
        (base_step + 1).astype(jnp.float32),
    )
    weight, moment_one, moment_two = adam_apply(
        weight, moment_one, moment_two, grad_two, norm_two, (base_step + 2).astype(jnp.float32)
    )
    return (weight, moment_one, moment_two)


def on_device(
    anchor, momentum, inner_weight, first_moment, second_moment, grad_first, grad_second, outer_step
):
    weight, moment_one, moment_two = inner_steps(
        inner_weight, first_moment, second_moment, grad_first, grad_second, outer_step
    )
    next_anchor, next_momentum = outer_update(anchor, momentum, inner_weight)
    next_inner = (next_anchor + (weight - inner_weight[0]))[None]
    return (next_anchor, next_momentum, next_inner, moment_one[None], moment_two[None])


def solution(mesh):
    fsdp = mesh.shape["fsdp"]
    split = Mesh(
        mesh.devices.reshape(2, mesh.shape["rep"] // 2, fsdp // 32, 8, 4),
        REP + FSDP,
    )
    return jax.shard_map(
        on_device,
        mesh=split,
        in_specs=(
            P(FSDP, None),
            P(FSDP, REP),
            P(REP, FSDP, None),
            P(REP, FSDP, None),
            P(REP, FSDP, None),
            P(REP, FSDP, None),
            P(REP, FSDP, None),
            P(),
        ),
        out_specs=(
            P(FSDP, None),
            P(FSDP, REP),
            P(REP, FSDP, None),
            P(REP, FSDP, None),
            P(REP, FSDP, None),
        ),
        check_vma=False,
    )
```

```python
import math

import jax
import jax.numpy as jnp
from jax import lax
from jax.sharding import Mesh
from jax.sharding import PartitionSpec as P

D = 3584
FF = 7168
REP = ("z_hi", "core")
FSDP = ("fsdp_0", "fsdp_1", "fsdp_2")


def all_summed(values, axes):
    count = 1
    for axis in axes:
        count *= lax.axis_size(axis)
    spread = jnp.broadcast_to(values[None], (count,) + values.shape)
    return lax.all_to_all(spread, axes, 0, 0, tiled=False).sum(axis=0)


def adam_apply(weight, first_moment, second_moment, grad_full, square_sum, step_count):
    factor = jnp.minimum(1.0, 0.5 * math.sqrt(D * FF) / (jnp.sqrt(square_sum) + 1e-06))
    scaled = factor * grad_full
    first_moment = 0.9 * first_moment + 0.1 * scaled
    second_moment = 0.95 * second_moment + 0.05 * scaled * scaled
    first_hat = first_moment / (1.0 - jnp.power(jnp.float32(0.9), step_count))
    second_hat = second_moment / (1.0 - jnp.power(jnp.float32(0.95), step_count))
    weight = weight - 0.1 * (first_hat / (jnp.sqrt(second_hat) + 1e-08) + 0.1 * weight)
    return (weight, first_moment, second_moment)


def outer_update(anchor, momentum, inner_weight):
    replicas = lax.axis_size("z_hi") * lax.axis_size("core")
    rows, cols = anchor.shape
    block = cols // replicas
    hi = lax.axis_index("z_hi")
    lo = lax.axis_index("core")

    def column(x, b):
        return lax.dynamic_slice_in_dim(x, b * block, block, 1)

    pseudo = anchor - inner_weight[0]
    kept = jnp.concatenate([column(pseudo, lo), column(pseudo, 2 + lo)], axis=1)
    given = jnp.concatenate([column(pseudo, 1 - lo), column(pseudo, 3 - lo)], axis=1)
    sibling = lax.all_gather(given, "core", axis=0, tiled=False)
    on_chip = kept + lax.dynamic_index_in_dim(sibling, 1 - lo, 0, keepdims=False)
    own_sum = column(on_chip, hi)
    other_sum = column(on_chip, 1 - hi)
    folded = column(anchor, 2 * hi + lo) - 0.567 * momentum - 0.3325 * own_sum
    payload = jnp.concatenate([folded, other_sum], axis=1)
    every = lax.all_gather(payload, REP, axis=0, tiled=False)
    next_anchor = jnp.concatenate(
        [
            every[b, :, :block] - 0.3325 * every[(b + 2) % 4, :, block:]
            for b in range(replicas)
        ],
        axis=1,
    )
    arrived = lax.dynamic_index_in_dim(every, 2 * (1 - hi) + lo, 0, keepdims=False)[:, block:]
    outer_grad = (own_sum + arrived) / replicas
    next_momentum = 0.9 * momentum + outer_grad
    return (next_anchor, next_momentum)


def inner_steps(inner_weight, first_moment, second_moment, grad_first, grad_second, outer_step):
    base_step = 2 * outer_step[0]
    both_grads = jnp.concatenate([grad_first, grad_second]).astype(jnp.float32)
    squares = jnp.sum(both_grads * both_grads, axis=(1, 2))
    grad_first, grad_second = lax.optimization_barrier((grad_first, grad_second))
    grad_one = grad_first[0].astype(jnp.float32)
    grad_two = grad_second[0].astype(jnp.float32)
    norm_one, norm_two = all_summed(squares, FSDP)
    weight, moment_one, moment_two = adam_apply(
        inner_weight[0],
        first_moment[0],
        second_moment[0],
        grad_one,
        norm_one,
        (base_step + 1).astype(jnp.float32),
    )
    weight, moment_one, moment_two = adam_apply(
        weight, moment_one, moment_two, grad_two, norm_two, (base_step + 2).astype(jnp.float32)
    )
    return (weight, moment_one, moment_two)


def on_device(
    anchor, momentum, inner_weight, first_moment, second_moment, grad_first, grad_second, outer_step
):
    weight, moment_one, moment_two = inner_steps(
        inner_weight, first_moment, second_moment, grad_first, grad_second, outer_step
    )
    next_anchor, next_momentum = outer_update(anchor, momentum, inner_weight)
    next_inner = (next_anchor + (weight - inner_weight[0]))[None]
    return (next_anchor, next_momentum, next_inner, moment_one[None], moment_two[None])


def solution(mesh):
    fsdp = mesh.shape["fsdp"]
    split = Mesh(
        mesh.devices.reshape(2, mesh.shape["rep"] // 2, fsdp // 32, 8, 4),
        REP + FSDP,
    )
    return jax.shard_map(
        on_device,
        mesh=split,
        in_specs=(
            P(FSDP, None),
            P(FSDP, REP),
            P(REP, FSDP, None),
            P(REP, FSDP, None),
            P(REP, FSDP, None),
            P(REP, FSDP, None),
            P(REP, FSDP, None),
            P(),
        ),
        out_specs=(
            P(FSDP, None),
            P(FSDP, REP),
            P(REP, FSDP, None),
            P(REP, FSDP, None),
            P(REP, FSDP, None),
        ),
        check_vma=False,
    )
```

```python
import math

import jax
import jax.numpy as jnp
from jax import lax
from jax.sharding import Mesh
from jax.sharding import PartitionSpec as P

D = 3584
FF = 7168
REP = ("z_hi", "core")
FSDP = ("fsdp_0", "fsdp_1", "fsdp_2")


def all_summed(values, axes):
    count = 1
    for axis in axes:
        count *= lax.axis_size(axis)
    spread = jnp.broadcast_to(values[None], (count,) + values.shape)
    return lax.all_to_all(spread, axes, 0, 0, tiled=False).sum(axis=0)


def adam_apply(weight, first_moment, second_moment, grad_full, square_sum, step_count):
    factor = jnp.minimum(1.0, 0.5 * math.sqrt(D * FF) / (jnp.sqrt(square_sum) + 1e-06))
    scaled = factor * grad_full
    first_moment = 0.9 * first_moment + 0.1 * scaled
    second_moment = 0.95 * second_moment + 0.05 * scaled * scaled
    first_hat = first_moment / (1.0 - jnp.power(jnp.float32(0.9), step_count))
    second_hat = second_moment / (1.0 - jnp.power(jnp.float32(0.95), step_count))
    weight = weight - 0.1 * (first_hat / (jnp.sqrt(second_hat) + 1e-08) + 0.1 * weight)
    return (weight, first_moment, second_moment)


def outer_update(anchor, momentum, inner_weight):
    replicas = lax.axis_size("z_hi") * lax.axis_size("core")
    rows, cols = anchor.shape
    block = cols // replicas
    hi = lax.axis_index("z_hi")
    lo = lax.axis_index("core")

    def column(x, b):
        return lax.dynamic_slice_in_dim(x, b * block, block, 1)

    pseudo = anchor - inner_weight[0]
    kept = jnp.stack([column(pseudo, lo), column(pseudo, 2 + lo)], axis=1)
    given = jnp.stack([column(pseudo, 1 - lo), column(pseudo, 3 - lo)], axis=1)
    sibling = lax.all_gather(given, "core", axis=0, tiled=False)
    on_chip = kept + lax.dynamic_index_in_dim(sibling, 1 - lo, 0, keepdims=False)
    own_sum = lax.dynamic_index_in_dim(on_chip, hi, 1, keepdims=False)
    other_sum = lax.dynamic_index_in_dim(on_chip, 1 - hi, 1, keepdims=False)
    folded = column(anchor, 2 * hi + lo) - 0.567 * momentum - 0.3325 * own_sum
    payload = jnp.stack([folded, other_sum], axis=1)
    every = lax.all_gather(payload, REP, axis=0, tiled=False)
    next_anchor = jnp.concatenate(
        [every[b, :, 0] - 0.3325 * every[(b + 2) % 4, :, 1] for b in range(replicas)], axis=1
    )
    arrived = lax.dynamic_index_in_dim(every, 2 * (1 - hi) + lo, 0, keepdims=False)[:, 1]
    outer_grad = (own_sum + arrived) / replicas
    next_momentum = 0.9 * momentum + outer_grad
    return (next_anchor, next_momentum)


def inner_steps(inner_weight, first_moment, second_moment, grad_first, grad_second, outer_step):
    base_step = 2 * outer_step[0]
    both_grads = jnp.concatenate([grad_first, grad_second]).astype(jnp.float32)
    squares = jnp.sum(both_grads * both_grads, axis=(1, 2))
    grad_first, grad_second = lax.optimization_barrier((grad_first, grad_second))
    grad_one = grad_first[0].astype(jnp.float32)
    grad_two = grad_second[0].astype(jnp.float32)
    norm_one, norm_two = all_summed(squares, FSDP)
    weight, moment_one, moment_two = adam_apply(
        inner_weight[0],
        first_moment[0],
        second_moment[0],
        grad_one,
        norm_one,
        (base_step + 1).astype(jnp.float32),
    )
    weight, moment_one, moment_two = adam_apply(
        weight, moment_one, moment_two, grad_two, norm_two, (base_step + 2).astype(jnp.float32)
    )
    return (weight, moment_one, moment_two)


def on_device(
    anchor, momentum, inner_weight, first_moment, second_moment, grad_first, grad_second, outer_step
):
    weight, moment_one, moment_two = inner_steps(
        inner_weight, first_moment, second_moment, grad_first, grad_second, outer_step
    )
    next_anchor, next_momentum = outer_update(anchor, momentum, inner_weight)
    next_inner = (next_anchor + (weight - inner_weight[0]))[None]
    return (next_anchor, next_momentum, next_inner, moment_one[None], moment_two[None])


def solution(mesh):
    fsdp = mesh.shape["fsdp"]
    split = Mesh(
        mesh.devices.reshape(2, mesh.shape["rep"] // 2, fsdp // 32, 8, 4),
        REP + FSDP,
    )
    return jax.shard_map(
        on_device,
        mesh=split,
        in_specs=(
            P(FSDP, None),
            P(FSDP, REP),
            P(REP, FSDP, None),
            P(REP, FSDP, None),
            P(REP, FSDP, None),
            P(REP, FSDP, None),
            P(REP, FSDP, None),
            P(),
        ),
        out_specs=(
            P(FSDP, None),
            P(FSDP, REP),
            P(REP, FSDP, None),
            P(REP, FSDP, None),
            P(REP, FSDP, None),
        ),
        check_vma=False,
    )
```

```python
import math

import jax
import jax.numpy as jnp
from jax import lax
from jax.sharding import Mesh
from jax.sharding import PartitionSpec as P

D = 3584
FF = 7168
REP = ("z_hi", "core")
FSDP = ("fsdp_0", "fsdp_1", "fsdp_2")


def all_summed(values, axes):
    count = 1
    for axis in axes:
        count *= lax.axis_size(axis)
    spread = jnp.broadcast_to(values[None], (count,) + values.shape)
    return lax.all_to_all(spread, axes, 0, 0, tiled=False).sum(axis=0)


def adam_apply(weight, first_moment, second_moment, grad_full, square_sum, step_count):
    factor = jnp.minimum(1.0, 0.5 * math.sqrt(D * FF) / (jnp.sqrt(square_sum) + 1e-06))
    scaled = factor * grad_full
    first_moment = 0.9 * first_moment + 0.1 * scaled
    second_moment = 0.95 * second_moment + 0.05 * scaled * scaled
    first_hat = first_moment / (1.0 - jnp.power(jnp.float32(0.9), step_count))
    second_hat = second_moment / (1.0 - jnp.power(jnp.float32(0.95), step_count))
    weight = weight - 0.1 * (first_hat / (jnp.sqrt(second_hat) + 1e-08) + 0.1 * weight)
    return (weight, first_moment, second_moment)


def outer_update(anchor, momentum, inner_weight):
    replicas = lax.axis_size("z_hi") * lax.axis_size("core")
    rows, cols = anchor.shape
    block = cols // replicas
    hi = lax.axis_index("z_hi")
    lo = lax.axis_index("core")
    pseudo = (anchor - inner_weight[0]).reshape(rows, 2, 2, block)
    kept = lax.dynamic_index_in_dim(pseudo, lo, 2, keepdims=False)
    given = lax.dynamic_index_in_dim(pseudo, 1 - lo, 2, keepdims=False)
    from_sibling = lax.dynamic_index_in_dim(
        lax.all_gather(given, "core", axis=0, tiled=False), 1 - lo, 0, keepdims=False
    )
    on_chip = kept + from_sibling
    anchor_half = lax.dynamic_index_in_dim(anchor.reshape(rows, 2, 2, block), lo, 2, keepdims=False)
    own_sum = lax.dynamic_index_in_dim(on_chip, hi, 1, keepdims=False)
    other_sum = lax.dynamic_index_in_dim(on_chip, 1 - hi, 1, keepdims=False)
    own_anchor = lax.dynamic_index_in_dim(anchor_half, hi, 1, keepdims=False)
    folded = own_anchor - 0.567 * momentum - 0.3325 * own_sum
    payload = jnp.stack([folded, other_sum], axis=1)
    every = lax.all_gather(payload, REP, axis=0, tiled=False).reshape(2, 2, rows, 2, block)
    next_anchor = jnp.concatenate(
        [every[b // 2, b % 2, :, 0] - 0.3325 * every[1 - b // 2, b % 2, :, 1] for b in range(replicas)],
        axis=1,
    )
    partner = lax.dynamic_index_in_dim(every, 1 - hi, 0, keepdims=False)
    arrived = lax.dynamic_index_in_dim(partner, lo, 0, keepdims=False)[:, 1]
    outer_grad = (own_sum + arrived) / replicas
    next_momentum = 0.9 * momentum + outer_grad
    return (next_anchor, next_momentum)


def inner_steps(inner_weight, first_moment, second_moment, grad_first, grad_second, outer_step):
    base_step = 2 * outer_step[0]
    grad_one = grad_first[0].astype(jnp.float32)
    grad_two = grad_second[0].astype(jnp.float32)
    both_grads = jnp.stack([grad_one, grad_two])
    squares = jnp.sum(both_grads * both_grads, axis=(1, 2))
    norm_one, norm_two = all_summed(squares, FSDP)
    weight, moment_one, moment_two = adam_apply(
        inner_weight[0],
        first_moment[0],
        second_moment[0],
        grad_one,
        norm_one,
        (base_step + 1).astype(jnp.float32),
    )
    weight, moment_one, moment_two = adam_apply(
        weight, moment_one, moment_two, grad_two, norm_two, (base_step + 2).astype(jnp.float32)
    )
    return (weight, moment_one, moment_two)


def on_device(
    anchor, momentum, inner_weight, first_moment, second_moment, grad_first, grad_second, outer_step
):
    weight, moment_one, moment_two = inner_steps(
        inner_weight, first_moment, second_moment, grad_first, grad_second, outer_step
    )
    next_anchor, next_momentum = outer_update(anchor, momentum, inner_weight)
    next_inner = (next_anchor + (weight - inner_weight[0]))[None]
    return (next_anchor, next_momentum, next_inner, moment_one[None], moment_two[None])


def solution(mesh):
    fsdp = mesh.shape["fsdp"]
    split = Mesh(
        mesh.devices.reshape(2, mesh.shape["rep"] // 2, fsdp // 32, 8, 4),
        REP + FSDP,
    )
    return jax.shard_map(
        on_device,
        mesh=split,
        in_specs=(
            P(FSDP, None),
            P(FSDP, REP),
            P(REP, FSDP, None),
            P(REP, FSDP, None),
            P(REP, FSDP, None),
            P(REP, FSDP, None),
            P(REP, FSDP, None),
            P(),
        ),
        out_specs=(
            P(FSDP, None),
            P(FSDP, REP),
            P(REP, FSDP, None),
            P(REP, FSDP, None),
            P(REP, FSDP, None),
        ),
        check_vma=False,
    )
```

```python
import math

import jax
import jax.numpy as jnp
from jax import lax
from jax.experimental.layout import Layout, with_layout_constraint
from jax.sharding import Mesh
from jax.sharding import PartitionSpec as P

D = 3584
FF = 7168
REP = ("z_hi", "core")
FSDP = ("fsdp_0", "fsdp_1", "fsdp_2")


def all_summed(values, axes):
    count = 1
    for axis in axes:
        count *= lax.axis_size(axis)
    spread = jnp.broadcast_to(values[None], (count,) + values.shape)
    return lax.all_to_all(spread, axes, 0, 0, tiled=False).sum(axis=0)


def adam_apply(weight, first_moment, second_moment, grad_full, square_sum, step_count):
    factor = jnp.minimum(1.0, 0.5 * math.sqrt(D * FF) / (jnp.sqrt(square_sum) + 1e-06))
    scaled = factor * grad_full
    first_moment = 0.9 * first_moment + 0.1 * scaled
    second_moment = 0.95 * second_moment + 0.05 * scaled * scaled
    first_hat = first_moment / (1.0 - jnp.power(jnp.float32(0.9), step_count))
    second_hat = second_moment / (1.0 - jnp.power(jnp.float32(0.95), step_count))
    weight = weight - 0.1 * (first_hat / (jnp.sqrt(second_hat) + 1e-08) + 0.1 * weight)
    return (weight, first_moment, second_moment)


def outer_update(anchor, momentum, inner_weight):
    replicas = lax.axis_size("z_hi") * lax.axis_size("core")
    rows, cols = anchor.shape
    block = cols // replicas
    hi = lax.axis_index("z_hi")
    lo = lax.axis_index("core")
    pseudo = (anchor - inner_weight[0]).reshape(rows, 2, 2, block)
    kept = lax.dynamic_index_in_dim(pseudo, lo, 2, keepdims=False)
    given = lax.dynamic_index_in_dim(pseudo, 1 - lo, 2, keepdims=False)
    from_sibling = lax.dynamic_index_in_dim(
        lax.all_gather(given, "core", axis=0, tiled=False), 1 - lo, 0, keepdims=False
    )
    on_chip = kept + from_sibling
    anchor_half = lax.dynamic_index_in_dim(anchor.reshape(rows, 2, 2, block), lo, 2, keepdims=False)
    own_sum = lax.dynamic_index_in_dim(on_chip, hi, 1, keepdims=False)
    other_sum = lax.dynamic_index_in_dim(on_chip, 1 - hi, 1, keepdims=False)
    own_anchor = lax.dynamic_index_in_dim(anchor_half, hi, 1, keepdims=False)
    folded = own_anchor - 0.567 * momentum - 0.3325 * own_sum
    payload = jnp.stack([folded, other_sum], axis=1)
    every = lax.all_gather(payload, REP, axis=0, tiled=False).reshape(2, 2, rows, 2, block)
    next_anchor = jnp.stack(
        [
            jnp.stack(
                [every[h, c, :, 0] - 0.3325 * every[1 - h, c, :, 1] for c in range(2)], axis=1
            )
            for h in range(2)
        ],
        axis=1,
    ).reshape(rows, cols)
    partner = lax.dynamic_index_in_dim(every, 1 - hi, 0, keepdims=False)
    arrived = lax.dynamic_index_in_dim(partner, lo, 0, keepdims=False)[:, 1]
    outer_grad = (own_sum + arrived) / replicas
    next_momentum = 0.9 * momentum + outer_grad
    return (next_anchor, next_momentum)


def inner_steps(inner_weight, first_moment, second_moment, grad_first, grad_second, outer_step):
    base_step = 2 * outer_step[0]
    grad_one = grad_first[0].astype(jnp.float32)
    grad_two = grad_second[0].astype(jnp.float32)
    both_grads = jnp.stack([grad_one, grad_two])
    squares = jnp.sum(both_grads * both_grads, axis=(1, 2))
    norm_one, norm_two = all_summed(squares, FSDP)
    weight, moment_one, moment_two = adam_apply(
        inner_weight[0],
        first_moment[0],
        second_moment[0],
        grad_one,
        norm_one,
        (base_step + 1).astype(jnp.float32),
    )
    weight, moment_one, moment_two = adam_apply(
        weight, moment_one, moment_two, grad_two, norm_two, (base_step + 2).astype(jnp.float32)
    )
    return (weight, moment_one, moment_two)


def on_device(
    anchor, momentum, inner_weight, first_moment, second_moment, grad_first, grad_second, outer_step
):
    weight, moment_one, moment_two = inner_steps(
        inner_weight, first_moment, second_moment, grad_first, grad_second, outer_step
    )
    next_anchor, next_momentum = outer_update(anchor, momentum, inner_weight)
    next_inner = (next_anchor + (weight - inner_weight[0]))[None]
    stored = Layout(major_to_minor=(1, 0, 2))
    next_inner, moment_one, moment_two = (
        with_layout_constraint(x, stored) for x in (next_inner, moment_one[None], moment_two[None])
    )
    return (next_anchor, next_momentum, next_inner, moment_one, moment_two)


def solution(mesh):
    fsdp = mesh.shape["fsdp"]
    split = Mesh(
        mesh.devices.reshape(2, mesh.shape["rep"] // 2, fsdp // 32, 8, 4),
        REP + FSDP,
    )
    return jax.shard_map(
        on_device,
        mesh=split,
        in_specs=(
            P(FSDP, None),
            P(FSDP, REP),
            P(REP, FSDP, None),
            P(REP, FSDP, None),
            P(REP, FSDP, None),
            P(REP, FSDP, None),
            P(REP, FSDP, None),
            P(),
        ),
        out_specs=(
            P(FSDP, None),
            P(FSDP, REP),
            P(REP, FSDP, None),
            P(REP, FSDP, None),
            P(REP, FSDP, None),
        ),
        check_vma=False,
    )
```

```python
import math

import jax
import jax.numpy as jnp
from jax import lax
from jax.sharding import Mesh
from jax.sharding import PartitionSpec as P

D = 3584
FF = 7168
REP = ("z_hi", "core")
FSDP = ("fsdp_0", "fsdp_1", "fsdp_2")


def all_summed(values, axes):
    count = 1
    for axis in axes:
        count *= lax.axis_size(axis)
    spread = jnp.broadcast_to(values[None], (count,) + values.shape)
    return lax.all_to_all(spread, axes, 0, 0, tiled=False).sum(axis=0)


def adam_apply(weight, first_moment, second_moment, grad_full, square_sum, step_count):
    factor = jnp.minimum(1.0, 0.5 * math.sqrt(D * FF) / (jnp.sqrt(square_sum) + 1e-06))
    scaled = factor * grad_full
    first_moment = 0.9 * first_moment + 0.1 * scaled
    second_moment = 0.95 * second_moment + 0.05 * scaled * scaled
    first_hat = first_moment / (1.0 - jnp.power(jnp.float32(0.9), step_count))
    second_hat = second_moment / (1.0 - jnp.power(jnp.float32(0.95), step_count))
    weight = weight - 0.1 * (first_hat / (jnp.sqrt(second_hat) + 1e-08) + 0.1 * weight)
    return (weight, first_moment, second_moment)


def outer_update(anchor, momentum, inner_weight):
    replicas = lax.axis_size("z_hi") * lax.axis_size("core")
    rows, cols = anchor.shape
    block = cols // replicas
    hi = lax.axis_index("z_hi")
    lo = lax.axis_index("core")
    pseudo = (anchor - inner_weight[0]).reshape(rows, 2, 2, block)
    kept = lax.dynamic_index_in_dim(pseudo, lo, 2, keepdims=False)
    given = lax.dynamic_index_in_dim(pseudo, 1 - lo, 2, keepdims=False)
    from_sibling = lax.dynamic_index_in_dim(
        lax.all_gather(given, "core", axis=0, tiled=False), 1 - lo, 0, keepdims=False
    )
    on_chip = kept + from_sibling
    anchor_half = lax.dynamic_index_in_dim(anchor.reshape(rows, 2, 2, block), lo, 2, keepdims=False)
    own_sum = lax.dynamic_index_in_dim(on_chip, hi, 1, keepdims=False)
    other_sum = lax.dynamic_index_in_dim(on_chip, 1 - hi, 1, keepdims=False)
    own_anchor = lax.dynamic_index_in_dim(anchor_half, hi, 1, keepdims=False)
    folded = own_anchor - 0.567 * momentum - 0.3325 * own_sum
    payload = jnp.stack([folded, other_sum], axis=1)
    every = lax.all_gather(payload, REP, axis=0, tiled=False).reshape(2, 2, rows, 2, block)
    next_anchor = jnp.stack(
        [
            jnp.stack(
                [every[h, c, :, 0] - 0.3325 * every[1 - h, c, :, 1] for c in range(2)], axis=1
            )
            for h in range(2)
        ],
        axis=1,
    ).reshape(rows, cols)
    partner = lax.dynamic_index_in_dim(every, 1 - hi, 0, keepdims=False)
    arrived = lax.dynamic_index_in_dim(partner, lo, 0, keepdims=False)[:, 1]
    outer_grad = (own_sum + arrived) / replicas
    next_momentum = 0.9 * momentum + outer_grad
    return (next_anchor, next_momentum)


def inner_steps(inner_weight, first_moment, second_moment, grad_first, grad_second, outer_step):
    base_step = 2 * outer_step[0]
    grad_one = grad_first[0].astype(jnp.float32)
    grad_two = grad_second[0].astype(jnp.float32)
    both_grads = jnp.stack([grad_one, grad_two])
    squares = jnp.sum(both_grads * both_grads, axis=(1, 2))
    norm_one, norm_two = all_summed(all_summed(squares, ("fsdp_0", "fsdp_2")), ("fsdp_1",))
    weight, moment_one, moment_two = adam_apply(
        inner_weight[0],
        first_moment[0],
        second_moment[0],
        grad_one,
        norm_one,
        (base_step + 1).astype(jnp.float32),
    )
    weight, moment_one, moment_two = adam_apply(
        weight, moment_one, moment_two, grad_two, norm_two, (base_step + 2).astype(jnp.float32)
    )
    return (weight, moment_one, moment_two)


def on_device(
    anchor, momentum, inner_weight, first_moment, second_moment, grad_first, grad_second, outer_step
):
    weight, moment_one, moment_two = inner_steps(
        inner_weight, first_moment, second_moment, grad_first, grad_second, outer_step
    )
    next_anchor, next_momentum = outer_update(anchor, momentum, inner_weight)
    next_inner = (next_anchor + (weight - inner_weight[0]))[None]
    return (next_anchor, next_momentum, next_inner, moment_one[None], moment_two[None])


def solution(mesh):
    fsdp = mesh.shape["fsdp"]
    split = Mesh(
        mesh.devices.reshape(2, mesh.shape["rep"] // 2, fsdp // 32, 8, 4),
        REP + FSDP,
    )
    return jax.shard_map(
        on_device,
        mesh=split,
        in_specs=(
            P(FSDP, None),
            P(FSDP, REP),
            P(REP, FSDP, None),
            P(REP, FSDP, None),
            P(REP, FSDP, None),
            P(REP, FSDP, None),
            P(REP, FSDP, None),
            P(),
        ),
        out_specs=(
            P(FSDP, None),
            P(FSDP, REP),
            P(REP, FSDP, None),
            P(REP, FSDP, None),
            P(REP, FSDP, None),
        ),
        check_vma=False,
    )
```

```python
import math

import jax
import jax.numpy as jnp
from jax import lax
from jax.sharding import Mesh
from jax.sharding import PartitionSpec as P

D = 3584
FF = 7168
REP = ("z_hi", "core")
FSDP = ("fsdp_0", "fsdp_1", "fsdp_2")


def all_summed(values, axes):
    count = 1
    for axis in axes:
        count *= lax.axis_size(axis)
    spread = jnp.broadcast_to(values[None], (count,) + values.shape)
    return lax.all_to_all(spread, axes, 0, 0, tiled=False).sum(axis=0)


def adam_apply(weight, first_moment, second_moment, grad_full, square_sum, step_count):
    factor = jnp.minimum(1.0, 0.5 * math.sqrt(D * FF) / (jnp.sqrt(square_sum) + 1e-06))
    scaled = factor * grad_full
    first_moment = 0.9 * first_moment + 0.1 * scaled
    second_moment = 0.95 * second_moment + 0.05 * scaled * scaled
    first_hat = first_moment / (1.0 - jnp.power(jnp.float32(0.9), step_count))
    second_hat = second_moment / (1.0 - jnp.power(jnp.float32(0.95), step_count))
    weight = weight - 0.1 * (first_hat / (jnp.sqrt(second_hat) + 1e-08) + 0.1 * weight)
    return (weight, first_moment, second_moment)


def outer_update(anchor, momentum, inner_weight):
    replicas = lax.axis_size("z_hi") * lax.axis_size("core")
    rows, cols = anchor.shape
    block = cols // replicas
    hi = lax.axis_index("z_hi")
    lo = lax.axis_index("core")
    pseudo = (anchor - inner_weight[0]).reshape(rows, 2, 2, block)
    kept = lax.dynamic_index_in_dim(pseudo, lo, 2, keepdims=False)
    given = lax.dynamic_index_in_dim(pseudo, 1 - lo, 2, keepdims=False)
    from_sibling = lax.dynamic_index_in_dim(
        lax.all_gather(given, "core", axis=0, tiled=False), 1 - lo, 0, keepdims=False
    )
    on_chip = kept + from_sibling
    anchor_half = lax.dynamic_index_in_dim(anchor.reshape(rows, 2, 2, block), lo, 2, keepdims=False)
    own_sum = lax.dynamic_index_in_dim(on_chip, hi, 1, keepdims=False)
    other_sum = lax.dynamic_index_in_dim(on_chip, 1 - hi, 1, keepdims=False)
    own_anchor = lax.dynamic_index_in_dim(anchor_half, hi, 1, keepdims=False)
    folded = own_anchor - 0.567 * momentum - 0.3325 * own_sum
    payload = jnp.stack([folded, other_sum], axis=1)
    every = lax.all_gather(payload, REP, axis=0, tiled=False).reshape(2, 2, rows, 2, block)
    next_anchor = jnp.stack(
        [
            jnp.stack(
                [every[h, c, :, 0] - 0.3325 * every[1 - h, c, :, 1] for c in range(2)], axis=1
            )
            for h in range(2)
        ],
        axis=1,
    ).reshape(rows, cols)
    partner = lax.dynamic_index_in_dim(every, 1 - hi, 0, keepdims=False)
    arrived = lax.dynamic_index_in_dim(partner, lo, 0, keepdims=False)[:, 1]
    outer_grad = (own_sum + arrived) / replicas
    next_momentum = 0.9 * momentum + outer_grad
    return (next_anchor, next_momentum)


def inner_steps(inner_weight, first_moment, second_moment, grad_first, grad_second, outer_step):
    base_step = 2 * outer_step[0]
    both_grads = jnp.concatenate([grad_first, grad_second]).astype(jnp.float32)
    squares = jnp.sum(both_grads * both_grads, axis=(1, 2))
    grad_first, grad_second = lax.optimization_barrier((grad_first, grad_second))
    grad_one = grad_first[0].astype(jnp.float32)
    grad_two = grad_second[0].astype(jnp.float32)
    norm_one, norm_two = all_summed(squares, FSDP)
    weight, moment_one, moment_two = adam_apply(
        inner_weight[0],
        first_moment[0],
        second_moment[0],
        grad_one,
        norm_one,
        (base_step + 1).astype(jnp.float32),
    )
    weight, moment_one, moment_two = adam_apply(
        weight, moment_one, moment_two, grad_two, norm_two, (base_step + 2).astype(jnp.float32)
    )
    return (weight, moment_one, moment_two)


def on_device(
    anchor, momentum, inner_weight, first_moment, second_moment, grad_first, grad_second, outer_step
):
    weight, moment_one, moment_two = inner_steps(
        inner_weight, first_moment, second_moment, grad_first, grad_second, outer_step
    )
    next_anchor, next_momentum = outer_update(anchor, momentum, inner_weight)
    next_inner = (next_anchor + (weight - inner_weight[0]))[None]
    return (next_anchor, next_momentum, next_inner, moment_one[None], moment_two[None])


def solution(mesh):
    fsdp = mesh.shape["fsdp"]
    split = Mesh(
        mesh.devices.reshape(2, mesh.shape["rep"] // 2, fsdp // 32, 8, 4),
        REP + FSDP,
    )
    return jax.shard_map(
        on_device,
        mesh=split,
        in_specs=(
            P(FSDP, None),
            P(FSDP, REP),
            P(REP, FSDP, None),
            P(REP, FSDP, None),
            P(REP, FSDP, None),
            P(REP, FSDP, None),
            P(REP, FSDP, None),
            P(),
        ),
        out_specs=(
            P(FSDP, None),
            P(FSDP, REP),
            P(REP, FSDP, None),
            P(REP, FSDP, None),
            P(REP, FSDP, None),
        ),
        check_vma=False,
    )
```
